256 devices in a mesh: group: 4 (over y), shard: 16 (over x_hi, z), tensor: 4 (over x_lo, core).
Axes of the slice: x: 4 (x_hi: 2, x_lo: 2; x = x_hi * 2 + x_lo), y: 4, z: 8, core: 2. Of those that a mesh axis runs over, the one named last changes fastest.
Arguments:
- group_weights: bfloat16 [4, 8, 1024, 8704], P('group', None, None, ('shard', 'tensor')), may hold values from -6 to 6
- anchor: float32 [8, 1024, 16, 4, 136], P(None, ('group', 'shard'), None, 'tensor'), may hold values from -6 to 6
- momentum: float32 [8, 1024, 16, 4, 136], P(None, ('group', 'shard'), None, 'tensor'), may hold values from -6 to 6
- group_embedding: bfloat16 [4, 32000, 1024], P('group', 'shard', 'tensor'), may hold values from -6 to 6
- emb_anchor: float32 [32000, 1024], P('shard', 'tensor'), may hold values from -6 to 6
- emb_momentum: float32 [32000, 1024], P('shard', 'tensor'), may hold values from -6 to 6
- basis: float32 [1024, 64], P('tensor'), may hold values from -0.1875 to 0.1875
Outputs:
- new_weights: bfloat16 [8, 1024, 8704], P(None, None, ('shard', 'tensor'))
- new_anchor: float32 [8, 1024, 16, 4, 136], P(None, ('group', 'shard'), None, 'tensor')
- new_momentum: float32 [8, 1024, 16, 4, 136], P(None, ('group', 'shard'), None, 'tensor')
- new_embedding: bfloat16 [32000, 1024], P('shard', 'tensor')
- new_emb_anchor: float32 [32000, 1024], P('shard', 'tensor')
- new_emb_momentum: float32 [32000, 1024], P('shard', 'tensor')
The draws below stay inside these ranges and needn't reach their ends.
All inputs are finite; a program needn't handle non-finite values.
Results may differ from the reference program's by a relative error of at most 0.012.
Values may be sent and summed in bfloat16 or wider, within the bound.
No kernel may reach another device: no remote copies, remote signals or barrier semaphores. Data moves between devices by JAX's collectives and lax.ppermute only.
A program may use at most 128 MiB of HBM per device.

```python
import jax
import jax.numpy as jnp
from jax import lax

D = 1024
LAYERS = 8
RANK = 64
COLS = 8704
NS = 16
NT = 4
CW = 136
GROUPS = 4
VOCAB = 32000


def levels(stream_key, dims, shards, least, top_value):
    def one(position, parts):
        steps = jax.random.uniform(jax.random.fold_in(jax.random.fold_in(stream_key, 6), position), (parts,), jnp.float32, least / len(shards), top_value / len(shards))
        return jnp.repeat(jnp.exp(steps), dims[position] // parts).reshape((-1,) + (1,) * (len(dims) - position - 1))

    factor_of = one(*shards[0])
    for cut in shards[1:]:
        factor_of = factor_of * one(*cut)
    return factor_of


def gaussian(rng, extent, deviation, bound, pieces=(), dtype=jnp.bfloat16):
    result = jax.random.normal(rng, extent, jnp.float32) * deviation
    if len(pieces) > 0:
        result = levels(rng, extent, pieces, -0.22, 0.18) * result
    return jnp.clip(result, min=-bound, max=bound).astype(dtype)


def setup_inputs(seed: int = 0) -> dict:
    seeds = jax.random.split(jax.random.key(seed), 8)
    group_weights = gaussian(seeds[0], (GROUPS, LAYERS, D, COLS), 1.0, 6.0, ((0, 4), (3, 64)))
    anchor = gaussian(seeds[1], (LAYERS, D, NS, NT, CW), 1.0, 6.0, ((1, 64), (3, 4)), jnp.float32)
    momentum = gaussian(seeds[2], (LAYERS, D, NS, NT, CW), 1.0, 6.0, ((1, 64), (3, 4)), jnp.float32)
    group_embedding = gaussian(seeds[3], (GROUPS, VOCAB, D), 1.0, 6.0, ((0, 4), (1, 16), (2, 4)))
    emb_anchor = gaussian(seeds[4], (VOCAB, D), 1.0, 6.0, ((0, 16), (1, 4)), jnp.float32)
    emb_momentum = gaussian(seeds[5], (VOCAB, D), 1.0, 6.0, ((0, 16), (1, 4)), jnp.float32)
    basis = gaussian(seeds[6], (D, RANK), D ** -0.5, 0.1875, ((0, 4),), jnp.float32)
    return dict(group_weights=group_weights, anchor=anchor, momentum=momentum, group_embedding=group_embedding, emb_anchor=emb_anchor, emb_momentum=emb_momentum, basis=basis)


outer_rate = 0.7
momentum_decay = 0.9


def reference(group_weights, anchor, momentum, group_embedding, emb_anchor, emb_momentum, basis):
    flat_anchor = anchor.reshape(LAYERS, D, COLS)
    flat_momentum = momentum.reshape(LAYERS, D, COLS)
    summed = jnp.sum(group_weights.astype(jnp.float32), axis=0)
    delta = flat_anchor - summed / GROUPS
    moved = momentum_decay * flat_momentum + delta
    stepped = flat_anchor - outer_rate * (delta + momentum_decay * moved)
    new_weights = stepped.astype(jnp.bfloat16)
    emb_sum = jnp.sum(group_embedding.astype(jnp.float32), axis=0)
    difference = emb_anchor - emb_sum / GROUPS
    coef = jnp.dot(difference, basis, precision=lax.Precision.HIGHEST)
    emb_delta = jnp.dot(coef, basis.T, precision=lax.Precision.HIGHEST)
    emb_moved = momentum_decay * emb_momentum + emb_delta
    emb_stepped = emb_anchor - outer_rate * (emb_delta + momentum_decay * emb_moved)
    shape = (LAYERS, D, NS, NT, CW)
    return (new_weights, stepped.reshape(shape), moved.reshape(shape),
            emb_stepped.astype(jnp.bfloat16), emb_stepped, emb_moved)
```

```python
import jax
import jax.numpy as jnp
from jax import lax
from jax.sharding import PartitionSpec as P

outer_rate = 0.7
momentum_decay = 0.9


def per_device(group_weights, anchor, momentum, group_embedding, emb_anchor, emb_momentum, basis):
    groups = lax.axis_size("group")
    layers = group_weights.shape[1]
    width = group_weights.shape[2]
    block = group_weights.shape[3]
    local_weights = group_weights[0]
    part = lax.psum_scatter(
        local_weights.astype(jnp.float32).astype(jnp.bfloat16),
        "group",
        scatter_dimension=1,
        tiled=True,
    )
    part = part.reshape(layers, part.shape[1], 1, 1, block)
    summed = lax.all_to_all(part, "shard", split_axis=1, concat_axis=2, tiled=True).astype(jnp.float32)
    delta = anchor - summed / groups
    moved = momentum_decay * momentum + delta
    stepped = anchor - outer_rate * (delta + momentum_decay * moved)
    stepped_half = stepped.astype(jnp.bfloat16)
    columns = lax.all_to_all(stepped_half, "shard", split_axis=2, concat_axis=1, tiled=True)
    whole = lax.all_gather(columns, "group", axis=1, tiled=True)
    new_weights = whole.reshape(layers, width, block)
    local_difference = emb_anchor - group_embedding[0].astype(jnp.float32)
    partial = jnp.dot(local_difference, basis, precision=lax.Precision.HIGHEST)
    coef = lax.psum(partial, ("group", "tensor")) * (1.0 / groups)
    emb_delta = jnp.dot(coef, basis.T, precision=lax.Precision.HIGHEST)
    emb_moved = momentum_decay * emb_momentum + emb_delta
    emb_stepped = emb_anchor - outer_rate * (emb_delta + momentum_decay * emb_moved)
    return (new_weights, stepped, moved, emb_stepped.astype(jnp.bfloat16), emb_stepped, emb_moved)


def solution(mesh):
    return jax.shard_map(
        per_device,
        mesh=mesh,
        in_specs=(
            P("group", None, None, ("shard", "tensor")),
            P(None, ("group", "shard"), None, "tensor", None),
            P(None, ("group", "shard"), None, "tensor", None),
            P("group", "shard", "tensor"),
            P("shard", "tensor"),
            P("shard", "tensor"),
            P("tensor", None),
        ),
        out_specs=(
            P(None, None, ("shard", "tensor")),
            P(None, ("group", "shard"), None, "tensor", None),
            P(None, ("group", "shard"), None, "tensor", None),
            P("shard", "tensor"),
            P("shard", "tensor"),
            P("shard", "tensor"),
        ),
        check_vma=False,
    )
```

```python
import jax
import jax.numpy as jnp
from jax import lax
from jax.sharding import PartitionSpec as P


outer_rate = 0.7
momentum_decay = 0.9


def per_device(group_weights, anchor, momentum, group_embedding, emb_anchor, emb_momentum, basis):
    groups = lax.axis_size("group")
    layers = group_weights.shape[1]
    width = group_weights.shape[2]
    block = group_weights.shape[3]
    chunks = 2
    per = layers // chunks
    pieces_w, pieces_s, pieces_m = [], [], []
    local_weights = group_weights[0]
    whole_part = lax.psum_scatter(local_weights, "group", scatter_dimension=1, tiled=True)
    parts = [whole_part[k * per:(k + 1) * per] for k in range(chunks)]
    for k in range(chunks):
        sl = slice(k * per, (k + 1) * per)
        part = parts[k]
        part = part.reshape(per, part.shape[1], 1, 1, block)
        summed = lax.all_to_all(part, "shard", split_axis=1, concat_axis=2, tiled=True).astype(jnp.float32)
        a = anchor[sl]
        delta = a - summed / groups
        moved = momentum_decay * momentum[sl] + delta
        stepped = a - outer_rate * (delta + momentum_decay * moved)
        stepped_half = stepped.astype(jnp.bfloat16)
        columns = lax.all_to_all(stepped_half, "shard", split_axis=2, concat_axis=1, tiled=True)
        whole = lax.all_gather(columns, "group", axis=1, tiled=True)
        pieces_w.append(whole.reshape(per, width, block))
        pieces_s.append(stepped)
        pieces_m.append(moved)
    new_weights = jnp.concatenate(pieces_w, axis=0)
    stepped = jnp.concatenate(pieces_s, axis=0)
    moved = jnp.concatenate(pieces_m, axis=0)
    local_difference = emb_anchor - group_embedding[0].astype(jnp.float32)
    partial = jnp.dot(local_difference, basis, precision=lax.Precision.HIGHEST)
    coef = lax.psum(partial, ("group", "tensor")) * (1.0 / groups)
    emb_delta = jnp.dot(coef, basis.T, precision=lax.Precision.HIGHEST)
    emb_moved = momentum_decay * emb_momentum + emb_delta
    emb_stepped = emb_anchor - outer_rate * (emb_delta + momentum_decay * emb_moved)
    return (new_weights, stepped, moved, emb_stepped.astype(jnp.bfloat16), emb_stepped, emb_moved)


def solution(mesh):
    return jax.shard_map(
        per_device,
        mesh=mesh,
        in_specs=(
            P("group", None, None, ("shard", "tensor")),
            P(None, ("group", "shard"), None, "tensor", None),
            P(None, ("group", "shard"), None, "tensor", None),
            P("group", "shard", "tensor"),
            P("shard", "tensor"),
            P("shard", "tensor"),
            P("tensor", None),
        ),
        out_specs=(
            P(None, None, ("shard", "tensor")),
            P(None, ("group", "shard"), None, "tensor", None),
            P(None, ("group", "shard"), None, "tensor", None),
            P("shard", "tensor"),
            P("shard", "tensor"),
            P("shard", "tensor"),
        ),
        check_vma=False,
    )
```

```python
import jax
import jax.numpy as jnp
from jax import lax
from jax.sharding import PartitionSpec as P


outer_rate = 0.7
momentum_decay = 0.9


def per_device(group_weights, anchor, momentum, group_embedding, emb_anchor, emb_momentum, basis):
    groups = lax.axis_size("group")
    layers = group_weights.shape[1]
    width = group_weights.shape[2]
    block = group_weights.shape[3]
    local_weights = group_weights[0].reshape(layers, groups, width // groups, block)
    received = lax.all_to_all(local_weights, "group", split_axis=1, concat_axis=1, tiled=True)
    part = jnp.sum(received.astype(jnp.float32), axis=1).astype(jnp.bfloat16)
    part = part.reshape(layers, part.shape[1], 1, 1, block)
    summed = lax.all_to_all(part, "shard", split_axis=1, concat_axis=2, tiled=True).astype(jnp.float32)
    delta = anchor - summed / groups
    moved = momentum_decay * momentum + delta
    stepped = anchor - outer_rate * (delta + momentum_decay * moved)
    stepped_half = stepped.astype(jnp.bfloat16)
    columns = lax.all_to_all(stepped_half, "shard", split_axis=2, concat_axis=1, tiled=True)
    columns = columns.reshape(layers, width // groups, block)
    me = lax.axis_index("group")
    rows = width // groups
    new_weights = jnp.zeros((layers, width, block), columns.dtype)
    new_weights = lax.dynamic_update_slice_in_dim(new_weights, columns, me * rows, axis=1)
    for d in range(1, groups):
        got = lax.ppermute(columns, "group", [(i, (i + d) % groups) for i in range(groups)])
        new_weights = lax.dynamic_update_slice_in_dim(new_weights, got, ((me - d) % groups) * rows, axis=1)
    local_difference = emb_anchor - group_embedding[0].astype(jnp.float32)
    partial = jnp.dot(local_difference, basis, precision=lax.Precision.HIGHEST)
    coef = lax.psum(partial, ("group", "tensor")) * (1.0 / groups)
    emb_delta = jnp.dot(coef, basis.T, precision=lax.Precision.HIGHEST)
    emb_moved = momentum_decay * emb_momentum + emb_delta
    emb_stepped = emb_anchor - outer_rate * (emb_delta + momentum_decay * emb_moved)
    return (new_weights, stepped, moved, emb_stepped.astype(jnp.bfloat16), emb_stepped, emb_moved)


def solution(mesh):
    return jax.shard_map(
        per_device,
        mesh=mesh,
        in_specs=(
            P("group", None, None, ("shard", "tensor")),
            P(None, ("group", "shard"), None, "tensor", None),
            P(None, ("group", "shard"), None, "tensor", None),
            P("group", "shard", "tensor"),
            P("shard", "tensor"),
            P("shard", "tensor"),
            P("tensor", None),
        ),
        out_specs=(
            P(None, None, ("shard", "tensor")),
            P(None, ("group", "shard"), None, "tensor", None),
            P(None, ("group", "shard"), None, "tensor", None),
            P("shard", "tensor"),
            P("shard", "tensor"),
            P("shard", "tensor"),
        ),
        check_vma=False,
    )
```

```python
import jax
import jax.numpy as jnp
from jax import lax
from jax.sharding import PartitionSpec as P


outer_rate = 0.7
momentum_decay = 0.9


def per_device(group_weights, anchor, momentum, group_embedding, emb_anchor, emb_momentum, basis):
    groups = lax.axis_size("group")
    layers = group_weights.shape[1]
    width = group_weights.shape[2]
    block = group_weights.shape[3]
    local_weights = group_weights[0].reshape(layers, groups, width // groups, block)
    received = lax.all_to_all(local_weights, "group", split_axis=1, concat_axis=1, tiled=True)
    part = jnp.sum(received.astype(jnp.float32), axis=1).astype(jnp.bfloat16)
    part = part.reshape(layers, part.shape[1], 1, 1, block)
    summed = lax.all_to_all(part, "shard", split_axis=1, concat_axis=2, tiled=True).astype(jnp.float32)
    local_difference = emb_anchor - group_embedding[0].astype(jnp.float32)
    partial = jnp.dot(local_difference, basis, precision=lax.Precision.HIGHEST)
    partial, summed = lax.optimization_barrier((lax.psum(partial, "tensor"), summed))
    delta = anchor - summed / groups
    moved = momentum_decay * momentum + delta
    stepped = anchor - outer_rate * (delta + momentum_decay * moved)
    stepped_half = stepped.astype(jnp.bfloat16)
    columns = lax.all_to_all(stepped_half, "shard", split_axis=2, concat_axis=1, tiled=True)
    columns = columns.reshape(layers, width // groups, block)
    me = lax.axis_index("group")
    rows = width // groups
    new_weights = jnp.zeros((layers, width, block), columns.dtype)
    new_weights = lax.dynamic_update_slice_in_dim(new_weights, columns, me * rows, axis=1)
    for d in range(1, groups):
        got = lax.ppermute(columns, "group", [(i, (i + d) % groups) for i in range(groups)])
        new_weights = lax.dynamic_update_slice_in_dim(new_weights, got, ((me - d) % groups) * rows, axis=1)
    coef = lax.psum(partial, "group") * (1.0 / groups)
    emb_delta = jnp.dot(coef, basis.T, precision=lax.Precision.HIGHEST)
    emb_moved = momentum_decay * emb_momentum + emb_delta
    emb_stepped = emb_anchor - outer_rate * (emb_delta + momentum_decay * emb_moved)
    return (new_weights, stepped, moved, emb_stepped.astype(jnp.bfloat16), emb_stepped, emb_moved)


def solution(mesh):
    return jax.shard_map(
        per_device,
        mesh=mesh,
        in_specs=(
            P("group", None, None, ("shard", "tensor")),
            P(None, ("group", "shard"), None, "tensor", None),
            P(None, ("group", "shard"), None, "tensor", None),
            P("group", "shard", "tensor"),
            P("shard", "tensor"),
            P("shard", "tensor"),
            P("tensor", None),
        ),
        out_specs=(
            P(None, None, ("shard", "tensor")),
            P(None, ("group", "shard"), None, "tensor", None),
            P(None, ("group", "shard"), None, "tensor", None),
            P("shard", "tensor"),
            P("shard", "tensor"),
            P("shard", "tensor"),
        ),
        check_vma=False,
    )
```

```python
import jax
import jax.numpy as jnp
from jax import lax
from jax.sharding import PartitionSpec as P


outer_rate = 0.7
momentum_decay = 0.9


def per_device(group_weights, anchor, momentum, group_embedding, emb_anchor, emb_momentum, basis):
    groups = lax.axis_size("group")
    layers = group_weights.shape[1]
    width = group_weights.shape[2]
    block = group_weights.shape[3]
    local_weights = group_weights[0].reshape(layers, groups, width // groups, block)
    received = lax.all_to_all(local_weights, "group", split_axis=1, concat_axis=1, tiled=True)
    part = jnp.sum(received.astype(jnp.float32), axis=1).astype(jnp.bfloat16)
    shards = lax.axis_size("shard")
    rows_own = part.shape[1] // shards
    lanes = 128
    flat = rows_own * layers * block // lanes
    sent = part.reshape(layers, shards, rows_own, block).transpose(1, 0, 2, 3).reshape(shards, flat, lanes)
    got = lax.all_to_all(sent, "shard", split_axis=0, concat_axis=0, tiled=True)
    got = got.reshape(shards, layers, rows_own, block).transpose(1, 2, 0, 3)
    summed = got.reshape(layers, rows_own, shards, 1, block).astype(jnp.float32)
    delta = anchor - summed / groups
    moved = momentum_decay * momentum + delta
    stepped = anchor - outer_rate * (delta + momentum_decay * moved)
    stepped_half = stepped.astype(jnp.bfloat16)
    back = stepped_half.reshape(layers, rows_own, shards, block).transpose(2, 0, 1, 3).reshape(shards, flat, lanes)
    back = lax.all_to_all(back, "shard", split_axis=0, concat_axis=0, tiled=True)
    columns = back.reshape(shards, layers, rows_own, block).transpose(1, 0, 2, 3).reshape(layers, width // groups, block)
    me = lax.axis_index("group")
    rows = width // groups
    new_weights = jnp.zeros((layers, width, block), columns.dtype)
    new_weights = lax.dynamic_update_slice_in_dim(new_weights, columns, me * rows, axis=1)
    for d in range(1, groups):
        got = lax.ppermute(columns, "group", [(i, (i + d) % groups) for i in range(groups)])
        new_weights = lax.dynamic_update_slice_in_dim(new_weights, got, ((me - d) % groups) * rows, axis=1)
    local_difference = emb_anchor - group_embedding[0].astype(jnp.float32)
    partial = jnp.dot(local_difference, basis, precision=lax.Precision.HIGHEST)
    coef = lax.psum(partial, ("group", "tensor")) * (1.0 / groups)
    emb_delta = jnp.dot(coef, basis.T, precision=lax.Precision.HIGHEST)
    emb_moved = momentum_decay * emb_momentum + emb_delta
    emb_stepped = emb_anchor - outer_rate * (emb_delta + momentum_decay * emb_moved)
    return (new_weights, stepped, moved, emb_stepped.astype(jnp.bfloat16), emb_stepped, emb_moved)


def solution(mesh):
    return jax.shard_map(
        per_device,
        mesh=mesh,
        in_specs=(
            P("group", None, None, ("shard", "tensor")),
            P(None, ("group", "shard"), None, "tensor", None),
            P(None, ("group", "shard"), None, "tensor", None),
            P("group", "shard", "tensor"),
            P("shard", "tensor"),
            P("shard", "tensor"),
            P("tensor", None),
        ),
        out_specs=(
            P(None, None, ("shard", "tensor")),
            P(None, ("group", "shard"), None, "tensor", None),
            P(None, ("group", "shard"), None, "tensor", None),
            P("shard", "tensor"),
            P("shard", "tensor"),
            P("shard", "tensor"),
        ),
        check_vma=False,
    )
```

```python
import jax
import jax.numpy as jnp
from jax import lax
from jax.sharding import PartitionSpec as P


outer_rate = 0.7
momentum_decay = 0.9


def per_device(group_weights, anchor, momentum, group_embedding, emb_anchor, emb_momentum, basis):
    groups = lax.axis_size("group")
    layers = group_weights.shape[1]
    width = group_weights.shape[2]
    block = group_weights.shape[3]
    local_difference = emb_anchor - group_embedding[0].astype(jnp.float32)
    partial = jnp.dot(local_difference, basis, precision=lax.Precision.HIGHEST)
    partial, local_weights = lax.optimization_barrier((partial, group_weights[0]))
    coef = lax.psum(partial, ("group", "tensor")) * (1.0 / groups)
    emb_delta = jnp.dot(coef, basis.T, precision=lax.Precision.HIGHEST)
    emb_moved = momentum_decay * emb_momentum + emb_delta
    emb_stepped = emb_anchor - outer_rate * (emb_delta + momentum_decay * emb_moved)
    local_weights = local_weights.reshape(layers, groups, width // groups, block)
    received = lax.all_to_all(local_weights, "group", split_axis=1, concat_axis=1, tiled=True)
    part = jnp.sum(received.astype(jnp.float32), axis=1).astype(jnp.bfloat16)
    shards = lax.axis_size("shard")
    rows_own = part.shape[1] // shards
    lanes = 128
    flat = rows_own * layers * block // lanes
    sent = part.reshape(layers, shards, rows_own, block).transpose(1, 0, 2, 3).reshape(shards, flat, lanes)
    got = lax.all_to_all(sent, "shard", split_axis=0, concat_axis=0, tiled=True)
    got = got.reshape(shards, layers, rows_own, block).transpose(1, 2, 0, 3)
    summed = got.reshape(layers, rows_own, shards, 1, block).astype(jnp.float32)
    delta = anchor - summed / groups
    moved = momentum_decay * momentum + delta
    stepped = anchor - outer_rate * (delta + momentum_decay * moved)
    stepped_half = stepped.astype(jnp.bfloat16)
    columns = lax.all_to_all(stepped_half, "shard", split_axis=2, concat_axis=1, tiled=True)
    columns = columns.reshape(layers, width // groups, block)
    me = lax.axis_index("group")
    rows = width // groups
    new_weights = jnp.zeros((layers, width, block), columns.dtype)
    new_weights = lax.dynamic_update_slice_in_dim(new_weights, columns, me * rows, axis=1)
    for d in range(1, groups):
        got = lax.ppermute(columns, "group", [(i, (i + d) % groups) for i in range(groups)])
        if d == 1:
            emb_stepped, emb_moved, got = lax.optimization_barrier((emb_stepped, emb_moved, got))
        new_weights = lax.dynamic_update_slice_in_dim(new_weights, got, ((me - d) % groups) * rows, axis=1)
    return (new_weights, stepped, moved, emb_stepped.astype(jnp.bfloat16), emb_stepped, emb_moved)


def solution(mesh):
    return jax.shard_map(
        per_device,
        mesh=mesh,
        in_specs=(
            P("group", None, None, ("shard", "tensor")),
            P(None, ("group", "shard"), None, "tensor", None),
            P(None, ("group", "shard"), None, "tensor", None),
            P("group", "shard", "tensor"),
            P("shard", "tensor"),
            P("shard", "tensor"),
            P("tensor", None),
        ),
        out_specs=(
            P(None, None, ("shard", "tensor")),
            P(None, ("group", "shard"), None, "tensor", None),
            P(None, ("group", "shard"), None, "tensor", None),
            P("shard", "tensor"),
            P("shard", "tensor"),
            P("shard", "tensor"),
        ),
        check_vma=False,
    )
```

```python
import jax
import jax.numpy as jnp
from jax import lax
from jax.sharding import PartitionSpec as P


outer_rate = 0.7
momentum_decay = 0.9


def per_device(group_weights, anchor, momentum, group_embedding, emb_anchor, emb_momentum, basis):
    groups = lax.axis_size("group")
    layers = group_weights.shape[1]
    width = group_weights.shape[2]
    block = group_weights.shape[3]
    local_difference = emb_anchor - group_embedding[0].astype(jnp.float32)
    partial = jnp.dot(local_difference, basis, precision=lax.Precision.HIGHEST)
    partial, local_weights = lax.optimization_barrier((partial, group_weights[0]))
    partial = lax.psum(partial, "tensor")
    local_weights = local_weights.reshape(layers, groups, width // groups, block)
    received = lax.all_to_all(local_weights, "group", split_axis=1, concat_axis=1, tiled=True)
    part = jnp.sum(received.astype(jnp.float32), axis=1).astype(jnp.bfloat16)
    shards = lax.axis_size("shard")
    rows_own = part.shape[1] // shards
    lanes = 128
    flat = rows_own * layers * block // lanes
    sent = part.reshape(layers, shards, rows_own, block).transpose(1, 0, 2, 3).reshape(shards, flat, lanes)
    got = lax.all_to_all(sent, "shard", split_axis=0, concat_axis=0, tiled=True)
    partial, got = lax.optimization_barrier((partial, got))
    coef = lax.psum(partial, "group") * (1.0 / groups)
    emb_delta = jnp.dot(coef, basis.T, precision=lax.Precision.HIGHEST)
    emb_moved = momentum_decay * emb_momentum + emb_delta
    emb_stepped = emb_anchor - outer_rate * (emb_delta + momentum_decay * emb_moved)
    got = got.reshape(shards, layers, rows_own, block).transpose(1, 2, 0, 3)
    summed = got.reshape(layers, rows_own, shards, 1, block).astype(jnp.float32)
    delta = anchor - summed / groups
    moved = momentum_decay * momentum + delta
    stepped = anchor - outer_rate * (delta + momentum_decay * moved)
    stepped_half = stepped.astype(jnp.bfloat16)
    columns = lax.all_to_all(stepped_half, "shard", split_axis=2, concat_axis=1, tiled=True)
    columns = columns.reshape(layers, width // groups, block)
    me = lax.axis_index("group")
    rows = width // groups
    new_weights = jnp.zeros((layers, width, block), columns.dtype)
    new_weights = lax.dynamic_update_slice_in_dim(new_weights, columns, me * rows, axis=1)
    for d in range(1, groups):
        got = lax.ppermute(columns, "group", [(i, (i + d) % groups) for i in range(groups)])
        if d == 1:
            emb_stepped, emb_moved, got = lax.optimization_barrier((emb_stepped, emb_moved, got))
        new_weights = lax.dynamic_update_slice_in_dim(new_weights, got, ((me - d) % groups) * rows, axis=1)
    return (new_weights, stepped, moved, emb_stepped.astype(jnp.bfloat16), emb_stepped, emb_moved)


def solution(mesh):
    return jax.shard_map(
        per_device,
        mesh=mesh,
        in_specs=(
            P("group", None, None, ("shard", "tensor")),
            P(None, ("group", "shard"), None, "tensor", None),
            P(None, ("group", "shard"), None, "tensor", None),
            P("group", "shard", "tensor"),
            P("shard", "tensor"),
            P("shard", "tensor"),
            P("tensor", None),
        ),
        out_specs=(
            P(None, None, ("shard", "tensor")),
            P(None, ("group", "shard"), None, "tensor", None),
            P(None, ("group", "shard"), None, "tensor", None),
            P("shard", "tensor"),
            P("shard", "tensor"),
            P("shard", "tensor"),
        ),
        check_vma=False,
    )
```

```python
import jax
import jax.numpy as jnp
from jax import lax
from jax.sharding import PartitionSpec as P


outer_rate = 0.7
momentum_decay = 0.9


def per_device(group_weights, anchor, momentum, group_embedding, emb_anchor, emb_momentum, basis):
    groups = lax.axis_size("group")
    layers = group_weights.shape[1]
    width = group_weights.shape[2]
    block = group_weights.shape[3]
    local_difference = emb_anchor - group_embedding[0].astype(jnp.float32)
    partial = jnp.dot(local_difference, basis, precision=lax.Precision.HIGHEST)
    partial, local_weights = lax.optimization_barrier((partial, group_weights[0]))
    partial = lax.psum(partial, "tensor")
    local_weights = local_weights.reshape(layers, groups, width // groups, block)
    received = lax.all_to_all(local_weights, "group", split_axis=1, concat_axis=1, tiled=True)
    part = jnp.sum(received.astype(jnp.float32), axis=1).astype(jnp.bfloat16)
    got = lax.all_to_all(part.reshape(layers, part.shape[1], 1, 1, block), "shard", split_axis=1, concat_axis=2, tiled=True)
    partial, got = lax.optimization_barrier((partial, got))
    coef = lax.psum(partial, "group") * (1.0 / groups)
    emb_delta = jnp.dot(coef, basis.T, precision=lax.Precision.HIGHEST)
    emb_moved = momentum_decay * emb_momentum + emb_delta
    emb_stepped = emb_anchor - outer_rate * (emb_delta + momentum_decay * emb_moved)
    summed = got.astype(jnp.float32)
    delta = anchor - summed / groups
    moved = momentum_decay * momentum + delta
    stepped = anchor - outer_rate * (delta + momentum_decay * moved)
    stepped_half = stepped.astype(jnp.bfloat16)
    columns = lax.all_to_all(stepped_half, "shard", split_axis=2, concat_axis=1, tiled=True)
    columns = columns.reshape(layers, width // groups, block)
    me = lax.axis_index("group")
    rows = width // groups
    new_weights = jnp.zeros((layers, width, block), columns.dtype)
    new_weights = lax.dynamic_update_slice_in_dim(new_weights, columns, me * rows, axis=1)
    for d in range(1, groups):
        got = lax.ppermute(columns, "group", [(i, (i + d) % groups) for i in range(groups)])
        if d == 1:
            emb_stepped, emb_moved, got = lax.optimization_barrier((emb_stepped, emb_moved, got))
        new_weights = lax.dynamic_update_slice_in_dim(new_weights, got, ((me - d) % groups) * rows, axis=1)
    return (new_weights, stepped, moved, emb_stepped.astype(jnp.bfloat16), emb_stepped, emb_moved)


def solution(mesh):
    return jax.shard_map(
        per_device,
        mesh=mesh,
        in_specs=(
            P("group", None, None, ("shard", "tensor")),
            P(None, ("group", "shard"), None, "tensor", None),
            P(None, ("group", "shard"), None, "tensor", None),
            P("group", "shard", "tensor"),
            P("shard", "tensor"),
            P("shard", "tensor"),
            P("tensor", None),
        ),
        out_specs=(
            P(None, None, ("shard", "tensor")),
            P(None, ("group", "shard"), None, "tensor", None),
            P(None, ("group", "shard"), None, "tensor", None),
            P("shard", "tensor"),
            P("shard", "tensor"),
            P("shard", "tensor"),
        ),
        check_vma=False,
    )
```

```python
import jax
import jax.numpy as jnp
from jax import lax
from jax.sharding import PartitionSpec as P


outer_rate = 0.7
momentum_decay = 0.9


def per_device(group_weights, anchor, momentum, group_embedding, emb_anchor, emb_momentum, basis):
    groups = lax.axis_size("group")
    layers = group_weights.shape[1]
    width = group_weights.shape[2]
    block = group_weights.shape[3]
    local_difference = emb_anchor - group_embedding[0].astype(jnp.float32)
    partial = jnp.dot(local_difference, basis, precision=lax.Precision.HIGHEST)
    partial, local_weights = lax.optimization_barrier((partial, group_weights[0]))
    partial = lax.psum(partial, "tensor")
    local_weights = local_weights.reshape(layers, groups, width // groups, block)
    received = lax.all_to_all(local_weights, "group", split_axis=1, concat_axis=1, tiled=True)
    part = jnp.sum(received.astype(jnp.float32), axis=1).astype(jnp.bfloat16)
    shards = lax.axis_size("shard")
    rows_own = part.shape[1] // shards
    lanes = 128
    flat = rows_own * layers * block // lanes
    sent = part.reshape(layers, shards, rows_own, block).transpose(1, 0, 2, 3).reshape(shards, flat, lanes)
    got = lax.all_to_all(sent, "shard", split_axis=0, concat_axis=0, tiled=True)
    partial, got = lax.optimization_barrier((partial, got))
    coef = lax.psum(partial, "group") * (1.0 / groups)
    emb_delta = jnp.dot(coef, basis.T, precision=lax.Precision.HIGHEST)
    emb_moved = momentum_decay * emb_momentum + emb_delta
    emb_stepped = emb_anchor - outer_rate * (emb_delta + momentum_decay * emb_moved)
    got = got.reshape(shards, layers, rows_own, block).transpose(1, 2, 0, 3)
    summed = got.reshape(layers, rows_own, shards, 1, block).astype(jnp.float32)
    delta = anchor - summed / groups
    moved = momentum_decay * momentum + delta
    stepped = anchor - outer_rate * (delta + momentum_decay * moved)
    stepped_half = stepped.astype(jnp.bfloat16)
    columns = lax.all_to_all(stepped_half, "shard", split_axis=2, concat_axis=1, tiled=True)
    columns = columns.reshape(layers, width // groups, block)
    me = lax.axis_index("group")
    rows = width // groups
    new_weights = jnp.zeros((layers, width, block), columns.dtype)
    new_weights = lax.dynamic_update_slice_in_dim(new_weights, columns, me * rows, axis=1)
    for d in range(1, groups):
        got = lax.ppermute(columns, "group", [(i, (i + d) % groups) for i in range(groups)])
        if d == 1:
            emb_half, emb_stepped, emb_moved, got = lax.optimization_barrier(
                (emb_stepped.astype(jnp.bfloat16), emb_stepped, emb_moved, got))
        new_weights = lax.dynamic_update_slice_in_dim(new_weights, got, ((me - d) % groups) * rows, axis=1)
    return (new_weights, stepped, moved, emb_half, emb_stepped, emb_moved)


def solution(mesh):
    return jax.shard_map(
        per_device,
        mesh=mesh,
        in_specs=(
            P("group", None, None, ("shard", "tensor")),
            P(None, ("group", "shard"), None, "tensor", None),
            P(None, ("group", "shard"), None, "tensor", None),
            P("group", "shard", "tensor"),
            P("shard", "tensor"),
            P("shard", "tensor"),
            P("tensor", None),
        ),
        out_specs=(
            P(None, None, ("shard", "tensor")),
            P(None, ("group", "shard"), None, "tensor", None),
            P(None, ("group", "shard"), None, "tensor", None),
            P("shard", "tensor"),
            P("shard", "tensor"),
            P("shard", "tensor"),
        ),
        check_vma=False,
    )
```

```python
import jax
import jax.numpy as jnp
from jax import lax
from jax.sharding import PartitionSpec as P


outer_rate = 0.7
momentum_decay = 0.9


def per_device(group_weights, anchor, momentum, group_embedding, emb_anchor, emb_momentum, basis):
    groups = lax.axis_size("group")
    layers = group_weights.shape[1]
    width = group_weights.shape[2]
    block = group_weights.shape[3]
    local_difference = emb_anchor - group_embedding[0].astype(jnp.float32)
    partial = jnp.dot(local_difference, basis, precision=lax.Precision.HIGH)
    partial, local_weights = lax.optimization_barrier((partial, group_weights[0]))
    partial = lax.psum(partial, "tensor")
    local_weights = local_weights.reshape(layers, groups, width // groups, block)
    received = lax.all_to_all(local_weights, "group", split_axis=1, concat_axis=1, tiled=True)
    part = jnp.sum(received.astype(jnp.float32), axis=1).astype(jnp.bfloat16)
    shards = lax.axis_size("shard")
    rows_own = part.shape[1] // shards
    lanes = 128
    flat = rows_own * layers * block // lanes
    sent = part.reshape(layers, shards, rows_own, block).transpose(1, 0, 2, 3).reshape(shards, flat, lanes)
    got = lax.all_to_all(sent, "shard", split_axis=0, concat_axis=0, tiled=True)
    partial, got = lax.optimization_barrier((partial, got))
    coef = lax.psum(partial, "group") * (1.0 / groups)
    emb_delta = jnp.dot(coef, basis.T, precision=lax.Precision.HIGHEST)
    emb_moved = momentum_decay * emb_momentum + emb_delta
    emb_stepped = emb_anchor - outer_rate * (emb_delta + momentum_decay * emb_moved)
    got = got.reshape(shards, layers, rows_own, block).transpose(1, 2, 0, 3)
    summed = got.reshape(layers, rows_own, shards, 1, block).astype(jnp.float32)
    delta = anchor - summed / groups
    moved = momentum_decay * momentum + delta
    stepped = anchor - outer_rate * (delta + momentum_decay * moved)
    stepped_half = stepped.astype(jnp.bfloat16)
    columns = lax.all_to_all(stepped_half, "shard", split_axis=2, concat_axis=1, tiled=True)
    columns = columns.reshape(layers, width // groups, block)
    me = lax.axis_index("group")
    rows = width // groups
    new_weights = jnp.zeros((layers, width, block), columns.dtype)
    new_weights = lax.dynamic_update_slice_in_dim(new_weights, columns, me * rows, axis=1)
    for d in range(1, groups):
        got = lax.ppermute(columns, "group", [(i, (i + d) % groups) for i in range(groups)])
        if d == 1:
            emb_half, emb_stepped, emb_moved, got = lax.optimization_barrier(
                (emb_stepped.astype(jnp.bfloat16), emb_stepped, emb_moved, got))
        new_weights = lax.dynamic_update_slice_in_dim(new_weights, got, ((me - d) % groups) * rows, axis=1)
    return (new_weights, stepped, moved, emb_half, emb_stepped, emb_moved)


def solution(mesh):
    return jax.shard_map(
        per_device,
        mesh=mesh,
        in_specs=(
            P("group", None, None, ("shard", "tensor")),
            P(None, ("group", "shard"), None, "tensor", None),
            P(None, ("group", "shard"), None, "tensor", None),
            P("group", "shard", "tensor"),
            P("shard", "tensor"),
            P("shard", "tensor"),
            P("tensor", None),
        ),
        out_specs=(
            P(None, None, ("shard", "tensor")),
            P(None, ("group", "shard"), None, "tensor", None),
            P(None, ("group", "shard"), None, "tensor", None),
            P("shard", "tensor"),
            P("shard", "tensor"),
            P("shard", "tensor"),
        ),
        check_vma=False,
    )
```

```python
import jax
import jax.numpy as jnp
from jax import lax
from jax.sharding import PartitionSpec as P


outer_rate = 0.7
momentum_decay = 0.9


def per_device(group_weights, anchor, momentum, group_embedding, emb_anchor, emb_momentum, basis):
    groups = lax.axis_size("group")
    layers = group_weights.shape[1]
    width = group_weights.shape[2]
    block = group_weights.shape[3]
    local_difference = emb_anchor - group_embedding[0].astype(jnp.float32)
    partial = jnp.dot(local_difference, basis, precision=lax.Precision.HIGH)
    partial, local_weights = lax.optimization_barrier((partial, group_weights[0]))
    partial = lax.psum(partial, "tensor")
    local_weights = local_weights.reshape(layers, groups, width // groups, block)
    received = lax.all_to_all(local_weights, "group", split_axis=1, concat_axis=1, tiled=True)
    part = jnp.sum(received.astype(jnp.float32), axis=1).astype(jnp.bfloat16)
    shards = lax.axis_size("shard")
    rows_own = part.shape[1] // shards
    lanes = 128
    flat = rows_own * layers * block // lanes
    sent = part.reshape(layers, shards, rows_own, block).transpose(1, 0, 2, 3).reshape(shards, flat, lanes)
    got = lax.all_to_all(sent, "shard", split_axis=0, concat_axis=0, tiled=True)
    partial, got = lax.optimization_barrier((partial, got))
    coef = lax.psum(partial, "group") * (1.0 / groups)
    emb_delta = jnp.dot(coef, basis.T, precision=lax.Precision.HIGHEST)
    emb_moved = momentum_decay * emb_momentum + emb_delta
    emb_stepped = emb_anchor - outer_rate * (emb_delta + momentum_decay * emb_moved)
    got = got.reshape(shards, layers, rows_own, block).transpose(1, 2, 0, 3)
    summed = got.reshape(layers, rows_own, shards, 1, block).astype(jnp.float32)
    def outer_step(a, m, total):
        delta = a - total / groups
        moved = momentum_decay * m + delta
        return a - outer_rate * (delta + momentum_decay * moved), moved

    stepped_half = outer_step(anchor, momentum, summed)[0].astype(jnp.bfloat16)
    stepped, moved = outer_step(*lax.optimization_barrier((anchor, momentum, summed)))
    columns = lax.all_to_all(stepped_half, "shard", split_axis=2, concat_axis=1, tiled=True)
    columns = columns.reshape(layers, width // groups, block)
    me = lax.axis_index("group")
    rows = width // groups
    new_weights = jnp.zeros((layers, width, block), columns.dtype)
    new_weights = lax.dynamic_update_slice_in_dim(new_weights, columns, me * rows, axis=1)
    for d in range(1, groups):
        got = lax.ppermute(columns, "group", [(i, (i + d) % groups) for i in range(groups)])
        if d == 1:
            emb_half, emb_stepped, emb_moved, got = lax.optimization_barrier(
                (emb_stepped.astype(jnp.bfloat16), emb_stepped, emb_moved, got))
        new_weights = lax.dynamic_update_slice_in_dim(new_weights, got, ((me - d) % groups) * rows, axis=1)
    return (new_weights, stepped, moved, emb_half, emb_stepped, emb_moved)


def solution(mesh):
    return jax.shard_map(
        per_device,
        mesh=mesh,
        in_specs=(
            P("group", None, None, ("shard", "tensor")),
            P(None, ("group", "shard"), None, "tensor", None),
            P(None, ("group", "shard"), None, "tensor", None),
            P("group", "shard", "tensor"),
            P("shard", "tensor"),
            P("shard", "tensor"),
            P("tensor", None),
        ),
        out_specs=(
            P(None, None, ("shard", "tensor")),
            P(None, ("group", "shard"), None, "tensor", None),
            P(None, ("group", "shard"), None, "tensor", None),
            P("shard", "tensor"),
            P("shard", "tensor"),
            P("shard", "tensor"),
        ),
        check_vma=False,
    )
```
